512 devices in a mesh: lon: 128 (over z, x, y_hi, core), lat: 4 (over y_lo).
Axes of the slice: x: 4, y: 8 (y_hi: 2, y_lo: 4; y = y_hi * 4 + y_lo), z: 8, core: 2. Of those that a mesh axis runs over, the one named last changes fastest.
Arguments:
- state: float32 [2, 4, 5760, 512], P(None, None, 'lon', 'lat'), may hold values from -6 to 6
- courant: float32 [2, 5760, 512], P(None, 'lon', 'lat'), may hold values from 1 to 34560
- band_mask: int32 [512], P('lat'), may hold values 0 or 1
Outputs:
- updated: float32 [2, 4, 5760, 512], P(None, None, 'lon', 'lat')
The draws below stay inside these ranges and needn't reach their ends.
All inputs are finite; a program needn't handle non-finite values. No bound on the sum of `band_mask` on one device may be relied on, other than what follows from the above.
Results may differ from the reference program's by a relative error of at most 0.00029.
Values sent between devices are 32-bit elements; how exact they have to be, the bound alone decides.
No kernel may reach another device: no remote copies, remote signals or barrier semaphores. Data moves between devices by JAX's collectives and lax.ppermute only.
A program may use at most 64 MiB of HBM per device.

```python
import jax
import jax.numpy as jnp
from jax import lax

VERTICAL_LAYERS = 2
ITERS = 2
MERIDIAN_POINTS = 5760
PARALLEL_CIRCLES = 512


def draw_courant(key, part):
    stochastic_seeds = jax.random.split(key, 5)
    slow_share = 0.5
    slow = jax.random.uniform(stochastic_seeds[0], (VERTICAL_LAYERS, 1, PARALLEL_CIRCLES), jnp.float32) < slow_share
    spot = jax.random.uniform(stochastic_seeds[1], (VERTICAL_LAYERS, 1, PARALLEL_CIRCLES), jnp.float32)
    fast_lo = jnp.log(30.0)
    fast_hi = jnp.log(MERIDIAN_POINTS / 2.0)
    slow_lo = jnp.log(MERIDIAN_POINTS / 2.0)
    slow_hi = jnp.log(3.0 * MERIDIAN_POINTS)
    parallel_speed = jnp.where(slow, jnp.exp(slow_lo + spot * (slow_hi - slow_lo)), jnp.exp(fast_lo + spot * (fast_hi - fast_lo)))
    decay_multiplier = jnp.exp(jax.random.uniform(stochastic_seeds[2], (VERTICAL_LAYERS, MERIDIAN_POINTS, PARALLEL_CIRCLES), jnp.float32, jnp.log(0.5), jnp.log(2.0)))
    repeated_passes = jax.random.uniform(stochastic_seeds[3], (VERTICAL_LAYERS, MERIDIAN_POINTS, PARALLEL_CIRCLES), jnp.float32) < 3.0 / MERIDIAN_POINTS
    tiny_offset = jax.random.uniform(stochastic_seeds[4], (VERTICAL_LAYERS, MERIDIAN_POINTS, PARALLEL_CIRCLES), jnp.float32, 1.0, 4.0)
    return jnp.where(repeated_passes, tiny_offset, parallel_speed * decay_multiplier).astype(jnp.float32)


def touch_ends(drawn, rng, smallest, high):
    longest = drawn.shape.index(max(drawn.shape))
    spots = []
    for shift in (0, 1):
        where = [jax.random.randint(jax.random.fold_in(rng, axis), (), 0, length) for axis, length in enumerate(drawn.shape)]
        where[longest] = (where[longest] + shift) % drawn.shape[longest]
        spots.append(tuple(where))
    return drawn.at[spots[0]].set(smallest).at[spots[1]].set(high)


def block_levels(key, dims, shards, least, top_value):
    def one(axis_at, shards_of):
        steps = jax.random.uniform(jax.random.fold_in(jax.random.fold_in(key, 6), axis_at), (shards_of,), jnp.float32, least / len(shards), top_value / len(shards))
        return jnp.repeat(jnp.exp(steps), dims[axis_at] // shards_of).reshape((-1,) + (1,) * (len(dims) - axis_at - 1))

    factor_of = one(*shards[0])
    for cut in shards[1:]:
        factor_of = factor_of * one(*cut)
    return factor_of


def noise(own_key, dims, spread, most, cuts=(), kind=jnp.bfloat16):
    gain = block_levels(own_key, dims, cuts, -0.22, 0.18) if cuts else 1.0
    values = jax.random.normal(own_key, dims, jnp.float32) * spread * gain
    return jnp.minimum(jnp.maximum(values, -most), most).astype(kind)


def setup_inputs(seed: int = 0) -> dict:
    seeds = jax.random.split(jax.random.key(seed), 4)
    state = noise(seeds[0], (VERTICAL_LAYERS, 4, MERIDIAN_POINTS, PARALLEL_CIRCLES), 1.0, 6.0, ((2, 128), (3, 4)), jnp.float32)
    courant = draw_courant(jax.random.fold_in(seeds[3], 71), 0)
    band_mask = touch_ends((jax.random.randint(seeds[2], (PARALLEL_CIRCLES,), 0, 4) < 3).astype(jnp.int32), jax.random.fold_in(seeds[2], 1), 0, 1)
    return dict(state=state, courant=courant, band_mask=band_mask)


def tendency(field, turning):
    half_cycle = field.shape[2] // 2
    flips = jnp.array([-1.0, -1.0, 1.0, 1.0], jnp.float32)[None, :, None]
    north_rim = jnp.roll(field[..., 0], half_cycle, axis=2) * flips
    south_rim = jnp.roll(field[..., -1], half_cycle, axis=2) * flips
    north_rows = jnp.concatenate([north_rim[..., None], field[..., :-1]], axis=3)
    south_rows = jnp.concatenate([field[..., 1:], south_rim[..., None]], axis=3)
    east_cells = jnp.roll(field, -1, axis=2)
    west_cells = jnp.roll(field, 1, axis=2)
    u_wind = field[:, 0:1]
    v_wind = field[:, 1:2]
    result = 0.1 * (east_cells + west_cells - 2.0 * field) + 0.1 * (north_rows + south_rows - 2.0 * field)
    result = result - 0.25 * v_wind * (north_rows - south_rows)
    coriolis = jnp.concatenate([turning * v_wind, -turning * u_wind, jnp.zeros_like(field[:, 2:])], axis=1)
    return result + coriolis


def zonal_solve(star, courant):
    inverse = 1.0 / (1.0 + courant)
    decay_multiplier = courant * inverse
    items = (jnp.moveaxis(star, 2, 0), jnp.moveaxis(decay_multiplier, 1, 0), jnp.moveaxis(inverse, 1, 0))

    def advance(carry, item):
        value, product = carry
        source, rate, weight = item
        value = rate[:, None, :] * value + source * weight[:, None, :]
        product = rate * product
        return (value, product), (value, product)

    start_value = jnp.zeros((star.shape[0], star.shape[1], star.shape[3]), jnp.float32)
    start_product = jnp.ones((star.shape[0], star.shape[3]), jnp.float32)
    (last_value, last_product), (values, products) = lax.scan(advance, (start_value, start_product), items)
    wrapped = last_value / (1.0 - last_product)[:, None, :]
    solved = values + products[:, :, None, :] * wrapped[None]
    return jnp.moveaxis(solved, 0, 2)


def reference(state, courant, band_mask):
    total_rows = state.shape[3]
    row_ids = jnp.arange(total_rows, dtype=jnp.int32)
    latitude = jnp.pi / 2 - (row_ids.astype(jnp.float32) + 0.5) * jnp.pi / total_rows
    turning = 0.5 * jnp.sin(latitude)
    in_band = (band_mask == 1)[None, None, None, :]
    estimate = state
    for sweep in range(ITERS):
        middle = 0.5 * (state + estimate)
        star = state + tendency(middle, turning)
        solved = zonal_solve(star, courant)
        estimate = jnp.where(in_band, solved, star)
    return estimate
```

```python
import jax
import jax.numpy as jnp
from jax import lax
from jax.sharding import PartitionSpec as P

ITERS = 2


def from_behind(value, axis, steps):
    count = lax.axis_size(axis)
    pairs = [(source, (source + steps) % count) for source in range(count)]
    return lax.ppermute(value, axis, pairs)


def shift_along(x, steps, axis, fill):
    pad_shape = list(x.shape)
    pad_shape[axis] = steps
    head = jnp.full(pad_shape, fill, x.dtype)
    body = lax.slice_in_dim(x, 0, x.shape[axis] - steps, axis=axis)
    return jnp.concatenate([head, body], axis=axis)


def block_rates(rate):
    steps = []
    span = 1
    while span < rate.shape[1]:
        steps.append((span, rate))
        rate = rate * shift_along(rate, span, 1, 1.0)
        span *= 2
    return steps, rate


def block_scan(steps, source):
    for span, rate in steps:
        source = source + rate[:, None] * shift_along(source, span, 2, 0.0)
    return source


def lon_rates(gain):
    count = lax.axis_size("lon")
    rounds = []
    window = gain
    excl = jnp.ones_like(gain)
    span = 1
    while span < count:
        rounds.append((span, window, excl))
        got = from_behind(window, "lon", span)
        excl = excl * got
        window = window * got
        span *= 2
    return rounds, excl


def inflow(rounds, excl, gain, ends):
    window = ends
    excl_b = jnp.zeros_like(ends)
    for span, rate_w, rate_e in rounds:
        got = from_behind(window, "lon", span)
        excl_b = rate_e[:, None] * got + excl_b
        window = rate_w[:, None] * got + window
    return (excl[:, None] * ends + excl_b) / (1.0 - excl * gain)[:, None]


def halo_tendency(field, turning, first_band, last_band, half_cycle):
    east = from_behind(field[:, :, 0, :], "lon", -1)
    west = from_behind(field[:, :, -1, :], "lon", 1)
    north = from_behind(field[..., -1], "lat", 1)
    south = from_behind(field[..., 0], "lat", -1)
    pole_send = jnp.where(first_band, field[..., 0], field[..., -1])
    across = from_behind(pole_send, "lon", half_cycle)
    flips = jnp.array([-1.0, -1.0, 1.0, 1.0], jnp.float32)[None, :, None]
    north = jnp.where(first_band, across * flips, north)
    south = jnp.where(last_band, across * flips, south)
    north_rows = jnp.concatenate([north[..., None], field[..., :-1]], axis=3)
    south_rows = jnp.concatenate([field[..., 1:], south[..., None]], axis=3)
    east_cells = jnp.concatenate([field[:, :, 1:], east[:, :, None]], axis=2)
    west_cells = jnp.concatenate([west[:, :, None], field[:, :, :-1]], axis=2)
    u_wind = field[:, 0:1]
    v_wind = field[:, 1:2]
    result = 0.1 * (east_cells + west_cells - 2.0 * field) + 0.1 * (
        north_rows + south_rows - 2.0 * field
    )
    result = result - 0.25 * v_wind * (north_rows - south_rows)
    coriolis = jnp.concatenate(
        [turning * v_wind, -turning * u_wind, jnp.zeros_like(field[:, 2:])], axis=1
    )
    return result + coriolis


def local(state, courant, band_mask):
    rows = state.shape[3]
    lat_index = lax.axis_index("lat")
    lat_count = lax.axis_size("lat")
    half_cycle = lax.axis_size("lon") // 2
    total_rows = rows * lat_count
    row_ids = lat_index * rows + jnp.arange(rows, dtype=jnp.int32)
    latitude = jnp.pi / 2 - (row_ids.astype(jnp.float32) + 0.5) * jnp.pi / total_rows
    turning = 0.5 * jnp.sin(latitude)
    first_band = lat_index == 0
    last_band = lat_index == lat_count - 1
    inverse = 1.0 / (1.0 + courant)
    rate = courant * inverse
    steps, carried = block_rates(rate)
    gain = carried[:, -1, :]
    rounds, excl = lon_rates(gain)
    in_band = (band_mask == 1)[None, None, None, :]
    estimate = state
    for sweep in range(ITERS):
        middle = 0.5 * (state + estimate)
        star = state + halo_tendency(middle, turning, first_band, last_band, half_cycle)
        partial_value = block_scan(steps, star * inverse[:, None])
        ends = partial_value[:, :, -1, :]
        entry = inflow(rounds, excl, gain, ends)
        solved = partial_value + carried[:, None] * entry[:, :, None, :]
        estimate = jnp.where(in_band, solved, star)
    return estimate


def solution(mesh):
    in_specs = (P(None, None, "lon", "lat"), P(None, "lon", "lat"), P("lat"))
    out_specs = P(None, None, "lon", "lat")
    return jax.shard_map(local, mesh=mesh, in_specs=in_specs, out_specs=out_specs, check_vma=False)
```

```python
import jax
import jax.numpy as jnp
from jax import lax
from jax.sharding import PartitionSpec as P

ITERS = 2
RADIX = 4


def from_behind(value, axis, steps):
    count = lax.axis_size(axis)
    pairs = [(source, (source + steps) % count) for source in range(count)]
    return lax.ppermute(value, axis, pairs)


def shift_along(x, steps, axis, fill):
    pad_shape = list(x.shape)
    pad_shape[axis] = steps
    head = jnp.full(pad_shape, fill, x.dtype)
    body = lax.slice_in_dim(x, 0, x.shape[axis] - steps, axis=axis)
    return jnp.concatenate([head, body], axis=axis)


def block_rates(rate):
    steps = []
    span = 1
    while span < rate.shape[1]:
        steps.append((span, rate))
        rate = rate * shift_along(rate, span, 1, 1.0)
        span *= 2
    return steps, rate


def block_scan(steps, source):
    for span, rate in steps:
        source = source + rate[:, None] * shift_along(source, span, 2, 0.0)
    return source


def scan_plan(count):
    plan = []
    span = 1
    while span < count:
        radix = min(RADIX, count // span)
        plan.append((span, radix))
        span *= radix
    assert span == count
    return plan


def lon_inflow(gain, ends, saved):
    count = lax.axis_size("lon")
    first = saved is None
    if first:
        saved = []
        rate_w, rate_e = gain, jnp.ones_like(gain)
    window, excl = ends, jnp.zeros_like(ends)
    for number, (span, radix) in enumerate(scan_plan(count)):
        if first:
            message = jnp.concatenate([window, rate_w[:, None]], axis=1)
        else:
            message = window
        got = [from_behind(message, "lon", span * j) for j in range(1, radix)]
        if first:
            rates = [g[:, -1] for g in got]
            got = [g[:, :-1] for g in got]
            saved.append((rate_w, rate_e, rates))
        else:
            rate_w, rate_e, rates = saved[number]
        joined_b = got[-1]
        joined_a = rates[-1]
        for j in range(len(got) - 2, -1, -1):
            joined_b = rates[j][:, None] * joined_b + got[j]
            joined_a = rates[j] * joined_a
        excl = rate_e[:, None] * joined_b + excl
        window = rate_w[:, None] * joined_b + window
        if first:
            rate_e = rate_e * joined_a
            rate_w = rate_w * joined_a
    if first:
        saved.append(rate_e)
    rate_e = saved[-1]
    entry = (rate_e[:, None] * ends + excl) / (1.0 - rate_e * gain)[:, None]
    return entry, saved


def halo_tendency(field, turning, lat_index, half_cycle):
    lon_count = lax.axis_size("lon")
    lat_count = lax.axis_size("lat")
    assert lat_count % 2 == 0
    east = from_behind(field[:, :, 0, :], "lon", -1)
    west = from_behind(field[:, :, -1, :], "lon", 1)
    top = field[..., 0]
    bottom = field[..., -1]
    odd = lat_index % 2 == 1
    pairs_a = []
    pairs_b = []
    for d in range(lon_count):
        for l in range(lat_count):
            me = d * lat_count + l
            if l % 2 == 0:
                pairs_a.append((me, d * lat_count + l + 1))
            else:
                pairs_a.append((me, d * lat_count + l - 1))
            if l == 0 or l == lat_count - 1:
                pairs_b.append((me, ((d + half_cycle) % lon_count) * lat_count + l))
            elif l % 2 == 1:
                pairs_b.append((me, d * lat_count + l + 1))
            else:
                pairs_b.append((me, d * lat_count + l - 1))
    got_a = lax.ppermute(jnp.where(odd, top, bottom), ("lon", "lat"), pairs_a)
    got_b = lax.ppermute(jnp.where(odd, bottom, top), ("lon", "lat"), pairs_b)
    flips = jnp.array([-1.0, -1.0, 1.0, 1.0], jnp.float32)[None, :, None]
    pole = (lat_index == 0) | (lat_index == lat_count - 1)
    got_b = jnp.where(pole, got_b * flips, got_b)
    north = jnp.where(odd, got_a, got_b)
    south = jnp.where(odd, got_b, got_a)
    north_rows = jnp.concatenate([north[..., None], field[..., :-1]], axis=3)
    south_rows = jnp.concatenate([field[..., 1:], south[..., None]], axis=3)
    east_cells = jnp.concatenate([field[:, :, 1:], east[:, :, None]], axis=2)
    west_cells = jnp.concatenate([west[:, :, None], field[:, :, :-1]], axis=2)
    u_wind = field[:, 0:1]
    v_wind = field[:, 1:2]
    result = 0.1 * (east_cells + west_cells - 2.0 * field) + 0.1 * (
        north_rows + south_rows - 2.0 * field
    )
    result = result - 0.25 * v_wind * (north_rows - south_rows)
    coriolis = jnp.concatenate(
        [turning * v_wind, -turning * u_wind, jnp.zeros_like(field[:, 2:])], axis=1
    )
    return result + coriolis


def local(state, courant, band_mask):
    rows = state.shape[3]
    lat_index = lax.axis_index("lat")
    lat_count = lax.axis_size("lat")
    half_cycle = lax.axis_size("lon") // 2
    total_rows = rows * lat_count
    row_ids = lat_index * rows + jnp.arange(rows, dtype=jnp.int32)
    latitude = jnp.pi / 2 - (row_ids.astype(jnp.float32) + 0.5) * jnp.pi / total_rows
    turning = 0.5 * jnp.sin(latitude)
    inverse = 1.0 / (1.0 + courant)
    rate = courant * inverse
    steps, carried = block_rates(rate)
    gain = carried[:, -1, :]
    in_band = (band_mask == 1)[None, None, None, :]
    estimate = state
    saved = None
    for sweep in range(ITERS):
        middle = 0.5 * (state + estimate)
        star = state + halo_tendency(middle, turning, lat_index, half_cycle)
        partial_value = block_scan(steps, star * inverse[:, None])
        ends = partial_value[:, :, -1, :]
        entry, saved = lon_inflow(gain, ends, saved)
        solved = partial_value + carried[:, None] * entry[:, :, None, :]
        estimate = jnp.where(in_band, solved, star)
    return estimate


def solution(mesh):
    in_specs = (P(None, None, "lon", "lat"), P(None, "lon", "lat"), P("lat"))
    out_specs = P(None, None, "lon", "lat")
    return jax.shard_map(local, mesh=mesh, in_specs=in_specs, out_specs=out_specs, check_vma=False)
```

```python
import jax
import jax.numpy as jnp
from jax import lax
from jax.sharding import Mesh, PartitionSpec as P

ITERS = 2
LON = ("lz", "lx", "lyc")


def axis_count(axis):
    names = axis if isinstance(axis, tuple) else (axis,)
    count = 1
    for name in names:
        count *= lax.axis_size(name)
    return count


def from_behind(value, axis, steps):
    count = axis_count(axis)
    pairs = [(source, (source + steps) % count) for source in range(count)]
    return lax.ppermute(value, axis, pairs)


def shift_along(x, steps, axis, fill):
    pad_shape = list(x.shape)
    pad_shape[axis] = steps
    head = jnp.full(pad_shape, fill, x.dtype)
    body = lax.slice_in_dim(x, 0, x.shape[axis] - steps, axis=axis)
    return jnp.concatenate([head, body], axis=axis)


def block_rates(rate):
    steps = []
    span = 1
    while span < rate.shape[1]:
        steps.append((span, rate))
        rate = rate * shift_along(rate, span, 1, 1.0)
        span *= 2
    return steps, rate


def block_scan(steps, source):
    for span, rate in steps:
        source = source + rate[:, None] * shift_along(source, span, 2, 0.0)
    return source


def compose(later, earlier):
    return (later[0] * earlier[0], later[0][:, None] * earlier[1] + later[1])


def gathered(maps, axis):
    count = lax.axis_size(axis)
    packed = jnp.concatenate([maps[1], maps[0][:, None]], axis=1)
    spread = jnp.broadcast_to(packed[None], (count,) + packed.shape)
    got = lax.all_to_all(spread, axis, 0, 0, tiled=False)
    return [(got[i][:, -1], got[i][:, :-1]) for i in range(count)]


def pick(options, index):
    rates = jnp.stack([o[0] for o in options])
    offsets = jnp.stack([o[1] for o in options])
    return (
        lax.dynamic_index_in_dim(rates, index, 0, False),
        lax.dynamic_index_in_dim(offsets, index, 0, False),
    )


def group_parts(members, index):
    count = len(members)
    ident = (jnp.ones_like(members[0][0]), jnp.zeros_like(members[0][1]))
    before = [ident]
    for i in range(1, count):
        before.append(compose(members[i - 1], before[-1]))
    after = [ident]
    for i in range(count - 2, -1, -1):
        after.insert(0, compose(after[0], members[i + 1]))
    total = compose(members[-1], before[-1])
    return total, pick(before, index), pick(after, index)


def cyclic_rest(members, index):
    count = len(members)
    options = []
    for g in range(count):
        rest = members[(g + 1) % count]
        for k in range(2, count):
            rest = compose(members[(g + k) % count], rest)
        options.append(rest)
    return pick(options, index)


def lon_inflow(own):
    members = gathered(own, "lyc")
    total_yc, pre_yc, suf_yc = group_parts(members, lax.axis_index("lyc"))
    groups = gathered(total_yc, "lx")
    total_x, pre_x, suf_x = group_parts(groups, lax.axis_index("lx"))
    circle = gathered(total_x, "lz")
    rest = cyclic_rest(circle, lax.axis_index("lz"))
    excl = compose(pre_yc, compose(pre_x, compose(rest, compose(suf_x, suf_yc))))
    rate, offset = own
    return (excl[0][:, None] * offset + excl[1]) / (1.0 - excl[0] * rate)[:, None]


def halo_tendency(field, turning, lat_index, half_cycle):
    lon_count = axis_count(LON)
    lat_count = lax.axis_size("lat")
    assert lat_count % 2 == 0
    east = from_behind(field[:, :, 0, :], LON, -1)
    west = from_behind(field[:, :, -1, :], LON, 1)
    top = field[..., 0]
    bottom = field[..., -1]
    odd = lat_index % 2 == 1
    pairs_a = []
    pairs_b = []
    for d in range(lon_count):
        for l in range(lat_count):
            me = d * lat_count + l
            if l % 2 == 0:
                pairs_a.append((me, d * lat_count + l + 1))
            else:
                pairs_a.append((me, d * lat_count + l - 1))
            if l == 0 or l == lat_count - 1:
                pairs_b.append((me, ((d + half_cycle) % lon_count) * lat_count + l))
            elif l % 2 == 1:
                pairs_b.append((me, d * lat_count + l + 1))
            else:
                pairs_b.append((me, d * lat_count + l - 1))
    got_a = lax.ppermute(jnp.where(odd, top, bottom), LON + ("lat",), pairs_a)
    got_b = lax.ppermute(jnp.where(odd, bottom, top), LON + ("lat",), pairs_b)
    flips = jnp.array([-1.0, -1.0, 1.0, 1.0], jnp.float32)[None, :, None]
    pole = (lat_index == 0) | (lat_index == lat_count - 1)
    got_b = jnp.where(pole, got_b * flips, got_b)
    north = jnp.where(odd, got_a, got_b)
    south = jnp.where(odd, got_b, got_a)
    north_rows = jnp.concatenate([north[..., None], field[..., :-1]], axis=3)
    south_rows = jnp.concatenate([field[..., 1:], south[..., None]], axis=3)
    east_cells = jnp.concatenate([field[:, :, 1:], east[:, :, None]], axis=2)
    west_cells = jnp.concatenate([west[:, :, None], field[:, :, :-1]], axis=2)
    u_wind = field[:, 0:1]
    v_wind = field[:, 1:2]
    result = 0.1 * (east_cells + west_cells - 2.0 * field) + 0.1 * (
        north_rows + south_rows - 2.0 * field
    )
    result = result - 0.25 * v_wind * (north_rows - south_rows)
    coriolis = jnp.concatenate(
        [turning * v_wind, -turning * u_wind, jnp.zeros_like(field[:, 2:])], axis=1
    )
    return result + coriolis


def local(state, courant, band_mask):
    rows = state.shape[3]
    lat_index = lax.axis_index("lat")
    lat_count = lax.axis_size("lat")
    half_cycle = axis_count(LON) // 2
    total_rows = rows * lat_count
    row_ids = lat_index * rows + jnp.arange(rows, dtype=jnp.int32)
    latitude = jnp.pi / 2 - (row_ids.astype(jnp.float32) + 0.5) * jnp.pi / total_rows
    turning = 0.5 * jnp.sin(latitude)
    inverse = 1.0 / (1.0 + courant)
    rate = courant * inverse
    steps, carried = block_rates(rate)
    gain = carried[:, -1, :]
    in_band = (band_mask == 1)[None, None, None, :]
    estimate = state
    for sweep in range(ITERS):
        middle = 0.5 * (state + estimate)
        star = state + halo_tendency(middle, turning, lat_index, half_cycle)
        partial_value = block_scan(steps, star * inverse[:, None])
        ends = partial_value[:, :, -1, :]
        entry = lon_inflow((gain, ends))
        solved = partial_value + carried[:, None] * entry[:, :, None, :]
        estimate = jnp.where(in_band, solved, star)
    return estimate


def solution(mesh):
    lon_count = mesh.shape["lon"]
    inner = 4
    split = Mesh(
        mesh.devices.reshape(lon_count // (inner * inner), inner, inner, mesh.shape["lat"]),
        ("lz", "lx", "lyc", "lat"),
    )
    in_specs = (P(None, None, LON, "lat"), P(None, LON, "lat"), P("lat"))
    out_specs = P(None, None, LON, "lat")
    return jax.shard_map(local, mesh=split, in_specs=in_specs, out_specs=out_specs, check_vma=False)
```

```python
import jax
import jax.numpy as jnp
from jax import lax
from jax.sharding import Mesh, PartitionSpec as P

ITERS = 2
LON = ("lz", "lx", "lyc")


def axis_count(axis):
    names = axis if isinstance(axis, tuple) else (axis,)
    count = 1
    for name in names:
        count *= lax.axis_size(name)
    return count


def from_behind(value, axis, steps):
    count = axis_count(axis)
    pairs = [(source, (source + steps) % count) for source in range(count)]
    return lax.ppermute(value, axis, pairs)


def shift_along(x, steps, axis, fill):
    pad_shape = list(x.shape)
    pad_shape[axis] = steps
    head = jnp.full(pad_shape, fill, x.dtype)
    body = lax.slice_in_dim(x, 0, x.shape[axis] - steps, axis=axis)
    return jnp.concatenate([head, body], axis=axis)


def block_rates(rate):
    steps = []
    span = 1
    while span < rate.shape[1]:
        steps.append((span, rate))
        rate = rate * shift_along(rate, span, 1, 1.0)
        span *= 2
    return steps, rate


def block_scan(steps, source):
    for span, rate in steps:
        source = source + rate[:, None] * shift_along(source, span, 2, 0.0)
    return source


def compose(later, earlier):
    return (later[0] * earlier[0], later[0][:, None] * earlier[1] + later[1])


def gathered(maps, axis):
    count = axis_count(axis)
    packed = jnp.concatenate([maps[1], maps[0][:, None]], axis=1)
    spread = jnp.broadcast_to(packed[None], (count,) + packed.shape)
    got = lax.all_to_all(spread, axis, 0, 0, tiled=False)
    return [(got[i][:, -1], got[i][:, :-1]) for i in range(count)]


def pick(options, index):
    rates = jnp.stack([o[0] for o in options])
    offsets = jnp.stack([o[1] for o in options])
    return (
        lax.dynamic_index_in_dim(rates, index, 0, False),
        lax.dynamic_index_in_dim(offsets, index, 0, False),
    )


def group_parts(members, index):
    count = len(members)
    ident = (jnp.ones_like(members[0][0]), jnp.zeros_like(members[0][1]))
    before = [ident]
    for i in range(1, count):
        before.append(compose(members[i - 1], before[-1]))
    after = [ident]
    for i in range(count - 2, -1, -1):
        after.insert(0, compose(after[0], members[i + 1]))
    total = compose(members[-1], before[-1])
    return total, pick(before, index), pick(after, index)


def cyclic_rest(members, index):
    count = len(members)
    options = []
    for g in range(count):
        rest = members[(g + 1) % count]
        for k in range(2, count):
            rest = compose(members[(g + k) % count], rest)
        options.append(rest)
    return pick(options, index)


def lon_inflow(own):
    members = gathered(own, ("lx", "lyc"))
    place = lax.axis_index("lx") * lax.axis_size("lyc") + lax.axis_index("lyc")
    total, before, after = group_parts(members, place)
    circle = gathered(total, "lz")
    rest = cyclic_rest(circle, lax.axis_index("lz"))
    excl = compose(before, compose(rest, after))
    rate, offset = own
    return (excl[0][:, None] * offset + excl[1]) / (1.0 - excl[0] * rate)[:, None]


def halo_tendency(field, turning, lat_index, half_cycle):
    lon_count = axis_count(LON)
    lat_count = lax.axis_size("lat")
    assert lat_count % 2 == 0
    east = from_behind(field[:, :, 0, :], LON, -1)
    west = from_behind(field[:, :, -1, :], LON, 1)
    top = field[..., 0]
    bottom = field[..., -1]
    odd = lat_index % 2 == 1
    pairs_a = []
    pairs_b = []
    for d in range(lon_count):
        for l in range(lat_count):
            me = d * lat_count + l
            if l % 2 == 0:
                pairs_a.append((me, d * lat_count + l + 1))
            else:
                pairs_a.append((me, d * lat_count + l - 1))
            if l == 0 or l == lat_count - 1:
                pairs_b.append((me, ((d + half_cycle) % lon_count) * lat_count + l))
            elif l % 2 == 1:
                pairs_b.append((me, d * lat_count + l + 1))
            else:
                pairs_b.append((me, d * lat_count + l - 1))
    got_a = lax.ppermute(jnp.where(odd, top, bottom), LON + ("lat",), pairs_a)
    got_b = lax.ppermute(jnp.where(odd, bottom, top), LON + ("lat",), pairs_b)
    flips = jnp.array([-1.0, -1.0, 1.0, 1.0], jnp.float32)[None, :, None]
    pole = (lat_index == 0) | (lat_index == lat_count - 1)
    got_b = jnp.where(pole, got_b * flips, got_b)
    north = jnp.where(odd, got_a, got_b)
    south = jnp.where(odd, got_b, got_a)
    north_rows = jnp.concatenate([north[..., None], field[..., :-1]], axis=3)
    south_rows = jnp.concatenate([field[..., 1:], south[..., None]], axis=3)
    east_cells = jnp.concatenate([field[:, :, 1:], east[:, :, None]], axis=2)
    west_cells = jnp.concatenate([west[:, :, None], field[:, :, :-1]], axis=2)
    u_wind = field[:, 0:1]
    v_wind = field[:, 1:2]
    result = 0.1 * (east_cells + west_cells - 2.0 * field) + 0.1 * (
        north_rows + south_rows - 2.0 * field
    )
    result = result - 0.25 * v_wind * (north_rows - south_rows)
    coriolis = jnp.concatenate(
        [turning * v_wind, -turning * u_wind, jnp.zeros_like(field[:, 2:])], axis=1
    )
    return result + coriolis


def local(state, courant, band_mask):
    rows = state.shape[3]
    lat_index = lax.axis_index("lat")
    lat_count = lax.axis_size("lat")
    half_cycle = axis_count(LON) // 2
    total_rows = rows * lat_count
    row_ids = lat_index * rows + jnp.arange(rows, dtype=jnp.int32)
    latitude = jnp.pi / 2 - (row_ids.astype(jnp.float32) + 0.5) * jnp.pi / total_rows
    turning = 0.5 * jnp.sin(latitude)
    inverse = 1.0 / (1.0 + courant)
    rate = courant * inverse
    steps, carried = block_rates(rate)
    gain = carried[:, -1, :]
    in_band = (band_mask == 1)[None, None, None, :]
    estimate = state
    for sweep in range(ITERS):
        middle = 0.5 * (state + estimate)
        star = state + halo_tendency(middle, turning, lat_index, half_cycle)
        partial_value = block_scan(steps, star * inverse[:, None])
        ends = partial_value[:, :, -1, :]
        entry = lon_inflow((gain, ends))
        solved = partial_value + carried[:, None] * entry[:, :, None, :]
        estimate = jnp.where(in_band, solved, star)
    return estimate


def solution(mesh):
    lon_count = mesh.shape["lon"]
    inner = 4
    split = Mesh(
        mesh.devices.reshape(lon_count // (inner * inner), inner, inner, mesh.shape["lat"]),
        ("lz", "lx", "lyc", "lat"),
    )
    in_specs = (P(None, None, LON, "lat"), P(None, LON, "lat"), P("lat"))
    out_specs = P(None, None, LON, "lat")
    return jax.shard_map(local, mesh=split, in_specs=in_specs, out_specs=out_specs, check_vma=False)
```

```python
import jax
import jax.numpy as jnp
from jax import lax
from jax.sharding import Mesh, PartitionSpec as P

ITERS = 2
LON = ("lz", "lx", "lyc")
GROUP = ("lx", "lyc")


def axis_count(axis):
    names = axis if isinstance(axis, tuple) else (axis,)
    count = 1
    for name in names:
        count *= lax.axis_size(name)
    return count


def from_behind(value, axis, steps):
    count = axis_count(axis)
    pairs = [(source, (source + steps) % count) for source in range(count)]
    return lax.ppermute(value, axis, pairs)


def shift_along(x, steps, axis, fill):
    pad_shape = list(x.shape)
    pad_shape[axis] = steps
    head = jnp.full(pad_shape, fill, x.dtype)
    body = lax.slice_in_dim(x, 0, x.shape[axis] - steps, axis=axis)
    return jnp.concatenate([head, body], axis=axis)


def block_rates(rate):
    steps = []
    span = 1
    while span < rate.shape[1]:
        steps.append((span, rate))
        rate = rate * shift_along(rate, span, 1, 1.0)
        span *= 2
    return steps, rate


def block_scan(steps, source):
    for span, rate in steps:
        source = source + rate[:, None] * shift_along(source, span, 2, 0.0)
    return source


def compose(later, earlier):
    return (later[0] * earlier[0], later[0][:, None] * earlier[1] + later[1])


def gathered(maps, axis):
    count = axis_count(axis)
    packed = jnp.concatenate([maps[1], maps[0][:, None]], axis=1)
    spread = jnp.broadcast_to(packed[None], (count,) + packed.shape)
    got = lax.all_to_all(spread, axis, 0, 0, tiled=False)
    return [(got[i][:, -1], got[i][:, :-1]) for i in range(count)]


def pick(options, index):
    rates = jnp.stack([o[0] for o in options])
    offsets = jnp.stack([o[1] for o in options])
    return (
        lax.dynamic_index_in_dim(rates, index, 0, False),
        lax.dynamic_index_in_dim(offsets, index, 0, False),
    )


def group_parts(members, index):
    count = len(members)
    ident = (jnp.ones_like(members[0][0]), jnp.zeros_like(members[0][1]))
    before = [ident]
    for i in range(1, count):
        before.append(compose(members[i - 1], before[-1]))
    after = [ident]
    for i in range(count - 2, -1, -1):
        after.insert(0, compose(after[0], members[i + 1]))
    total = compose(members[-1], before[-1])
    return total, pick(before, index), pick(after, index)


def cyclic_rest(members, index):
    count = len(members)
    options = []
    for g in range(count):
        rest = members[(g + 1) % count]
        for k in range(2, count):
            rest = compose(members[(g + k) % count], rest)
        options.append(rest)
    return pick(options, index)


def fixed_point(excl, own):
    rate, offset = own
    return (excl[0][:, None] * offset + excl[1]) / (1.0 - excl[0] * rate)[:, None]


def group_place():
    return lax.axis_index("lx") * lax.axis_size("lyc") + lax.axis_index("lyc")


def lon_inflow(own):
    total, before, after = group_parts(gathered(own, GROUP), group_place())
    rest = cyclic_rest(gathered(total, "lz"), lax.axis_index("lz"))
    return fixed_point(compose(before, compose(rest, after)), own)


def lat_exchange(top, bottom, lat_index, half_cycle):
    lon_count = axis_count(LON)
    lat_count = lax.axis_size("lat")
    assert lat_count % 2 == 0
    odd = lat_index % 2 == 1
    pairs_a = []
    pairs_b = []
    for d in range(lon_count):
        for l in range(lat_count):
            me = d * lat_count + l
            if l % 2 == 0:
                pairs_a.append((me, d * lat_count + l + 1))
            else:
                pairs_a.append((me, d * lat_count + l - 1))
            if l == 0 or l == lat_count - 1:
                pairs_b.append((me, ((d + half_cycle) % lon_count) * lat_count + l))
            elif l % 2 == 1:
                pairs_b.append((me, d * lat_count + l + 1))
            else:
                pairs_b.append((me, d * lat_count + l - 1))
    got_a = lax.ppermute(jnp.where(odd, top, bottom), LON + ("lat",), pairs_a)
    got_b = lax.ppermute(jnp.where(odd, bottom, top), LON + ("lat",), pairs_b)
    pole = (lat_index == 0) | (lat_index == lat_count - 1)
    got_b = jnp.where(pole, got_b * flips()[None, :, None], got_b)
    return jnp.where(odd, got_a, got_b), jnp.where(odd, got_b, got_a)


def flips():
    return jnp.array([-1.0, -1.0, 1.0, 1.0], jnp.float32)


def stencil(field, north, south, east, west, turning):
    north_rows = jnp.concatenate([north[..., None], field[..., :-1]], axis=3)
    south_rows = jnp.concatenate([field[..., 1:], south[..., None]], axis=3)
    east_cells = jnp.concatenate([field[:, :, 1:], east[:, :, None]], axis=2)
    west_cells = jnp.concatenate([west[:, :, None], field[:, :, :-1]], axis=2)
    u_wind = field[:, 0:1]
    v_wind = field[:, 1:2]
    result = 0.1 * (east_cells + west_cells - 2.0 * field) + 0.1 * (
        north_rows + south_rows - 2.0 * field
    )
    result = result - 0.25 * v_wind * (north_rows - south_rows)
    coriolis = jnp.concatenate(
        [turning * v_wind, -turning * u_wind, jnp.zeros_like(field[:, 2:])], axis=1
    )
    return result + coriolis


def local(state, courant, band_mask):
    levels, comps, cols, rows = state.shape
    lat_index = lax.axis_index("lat")
    lat_count = lax.axis_size("lat")
    z_index = lax.axis_index("lz")
    z_count = lax.axis_size("lz")
    assert z_count % 2 == 0 and ITERS == 2
    half_cycle = axis_count(LON) // 2
    total_rows = rows * lat_count
    row_ids = lat_index * rows + jnp.arange(rows, dtype=jnp.int32)
    latitude = jnp.pi / 2 - (row_ids.astype(jnp.float32) + 0.5) * jnp.pi / total_rows
    turning = 0.5 * jnp.sin(latitude)
    inverse = 1.0 / (1.0 + courant)
    rate = courant * inverse
    steps, carried = block_rates(rate)
    gain = carried[:, -1, :]
    band = band_mask == 1
    in_band = band[None, None, None, :]

    edge_rates = jnp.stack([rate[:, 0, :], inverse[:, 0, :]], axis=1)
    got_east = from_behind(jnp.concatenate([state[:, :, 0, :], edge_rates], axis=1), LON, -1)
    east, east_rates = got_east[:, :comps], got_east[:, comps:]
    west = from_behind(state[:, :, -1, :], LON, 1)
    north, south = lat_exchange(state[..., 0], state[..., -1], lat_index, half_cycle)
    star = state + stencil(state, north, south, east, west, turning)
    star_east = from_behind(star[:, :, 0, :], LON, -1)
    star_west = from_behind(star[:, :, -1, :], LON, 1)
    partial = block_scan(steps, star * inverse[:, None])
    own = (gain, partial[:, :, -1, :])
    entry = lon_inflow(own)
    estimate = jnp.where(in_band, partial + carried[:, None] * entry[:, :, None, :], star)

    band_col = band[None, None, :]
    west = 0.5 * (west + jnp.where(band_col, entry, star_west))
    carry_in = estimate[:, :, -1, :]
    east_value = east_rates[:, 0:1] * carry_in + east_rates[:, 1:2] * star_east
    east = 0.5 * (east + jnp.where(band_col, east_value, star_east))
    middle = 0.5 * (state + estimate)
    north, south = lat_exchange(middle[..., 0], middle[..., -1], lat_index, half_cycle)

    for sweep in range(1, ITERS):
        star = state + stencil(middle, north, south, east, west, turning)
        partial = block_scan(steps, star * inverse[:, None])
        own = (gain, partial[:, :, -1, :])
        entry = lon_inflow(own)
        estimate = jnp.where(in_band, partial + carried[:, None] * entry[:, :, None, :], star)
    return estimate


def solution(mesh):
    lon_count = mesh.shape["lon"]
    inner = 4
    split = Mesh(
        mesh.devices.reshape(lon_count // (inner * inner), inner, inner, mesh.shape["lat"]),
        ("lz", "lx", "lyc", "lat"),
    )
    in_specs = (P(None, None, LON, "lat"), P(None, LON, "lat"), P("lat"))
    out_specs = P(None, None, LON, "lat")
    return jax.shard_map(local, mesh=split, in_specs=in_specs, out_specs=out_specs, check_vma=False)
```

```python
import jax
import jax.numpy as jnp
from jax import lax
from jax.sharding import Mesh, PartitionSpec as P

ITERS = 2
LON = ("lz", "lx", "lyc")
GROUP = ("lx", "lyc")


def axis_count(axis):
    names = axis if isinstance(axis, tuple) else (axis,)
    count = 1
    for name in names:
        count *= lax.axis_size(name)
    return count


def from_behind(value, axis, steps):
    count = axis_count(axis)
    pairs = [(source, (source + steps) % count) for source in range(count)]
    return lax.ppermute(value, axis, pairs)


def shift_along(x, steps, axis, fill):
    pad_shape = list(x.shape)
    pad_shape[axis] = steps
    head = jnp.full(pad_shape, fill, x.dtype)
    body = lax.slice_in_dim(x, 0, x.shape[axis] - steps, axis=axis)
    return jnp.concatenate([head, body], axis=axis)


def block_rates(rate):
    steps = []
    span = 1
    while span < rate.shape[1]:
        steps.append((span, rate))
        rate = rate * shift_along(rate, span, 1, 1.0)
        span *= 2
    return steps, rate


def block_scan(steps, source):
    for span, rate in steps:
        source = source + rate[:, None] * shift_along(source, span, 2, 0.0)
    return source


def compose(later, earlier):
    return (later[0] * earlier[0], later[0][:, None] * earlier[1] + later[1])


def gathered(maps, axis):
    count = axis_count(axis)
    packed = jnp.concatenate([maps[1], maps[0][:, None]], axis=1)
    spread = jnp.broadcast_to(packed[None], (count,) + packed.shape)
    got = lax.all_to_all(spread, axis, 0, 0, tiled=False)
    return [(got[i][:, -1], got[i][:, :-1]) for i in range(count)]


def pick(options, index):
    rate, offset = options[0]
    for number in range(1, len(options)):
        chosen = index == number
        rate = jnp.where(chosen, options[number][0], rate)
        offset = jnp.where(chosen, options[number][1], offset)
    return rate, offset


def group_parts(members, index):
    count = len(members)
    ident = (jnp.ones_like(members[0][0]), jnp.zeros_like(members[0][1]))
    before = [ident]
    for i in range(1, count):
        before.append(compose(members[i - 1], before[-1]))
    after = [ident]
    for i in range(count - 2, -1, -1):
        after.insert(0, compose(after[0], members[i + 1]))
    total = compose(members[-1], before[-1])
    return total, pick(before, index), pick(after, index)


def cyclic_rest(members, index):
    count = len(members)
    options = []
    for g in range(count):
        rest = members[(g + 1) % count]
        for k in range(2, count):
            rest = compose(members[(g + k) % count], rest)
        options.append(rest)
    return pick(options, index)


def fixed_point(excl, own):
    rate, offset = own
    return (excl[0][:, None] * offset + excl[1]) / (1.0 - excl[0] * rate)[:, None]


def group_place():
    return lax.axis_index("lx") * lax.axis_size("lyc") + lax.axis_index("lyc")


def lon_inflow(own):
    total, before, after = group_parts(gathered(own, GROUP), group_place())
    rest = cyclic_rest(gathered(total, "lz"), lax.axis_index("lz"))
    return fixed_point(compose(before, compose(rest, after)), own)


def lat_exchange(top, bottom, lat_index, half_cycle):
    lon_count = axis_count(LON)
    lat_count = lax.axis_size("lat")
    assert lat_count % 2 == 0
    odd = lat_index % 2 == 1
    pairs_a = []
    pairs_b = []
    for d in range(lon_count):
        for l in range(lat_count):
            me = d * lat_count + l
            if l % 2 == 0:
                pairs_a.append((me, d * lat_count + l + 1))
            else:
                pairs_a.append((me, d * lat_count + l - 1))
            if l == 0 or l == lat_count - 1:
                pairs_b.append((me, ((d + half_cycle) % lon_count) * lat_count + l))
            elif l % 2 == 1:
                pairs_b.append((me, d * lat_count + l + 1))
            else:
                pairs_b.append((me, d * lat_count + l - 1))
    got_a = lax.ppermute(jnp.where(odd, top, bottom), LON + ("lat",), pairs_a)
    got_b = lax.ppermute(jnp.where(odd, bottom, top), LON + ("lat",), pairs_b)
    pole = (lat_index == 0) | (lat_index == lat_count - 1)
    got_b = jnp.where(pole, got_b * flips()[None, :, None], got_b)
    return jnp.where(odd, got_a, got_b), jnp.where(odd, got_b, got_a)


def flips():
    return jnp.array([-1.0, -1.0, 1.0, 1.0], jnp.float32)


def stencil(field, north, south, east, west, turning):
    north_rows = jnp.concatenate([north[..., None], field[..., :-1]], axis=3)
    south_rows = jnp.concatenate([field[..., 1:], south[..., None]], axis=3)
    east_cells = jnp.concatenate([field[:, :, 1:], east[:, :, None]], axis=2)
    west_cells = jnp.concatenate([west[:, :, None], field[:, :, :-1]], axis=2)
    u_wind = field[:, 0:1]
    v_wind = field[:, 1:2]
    result = 0.1 * (east_cells + west_cells - 2.0 * field) + 0.1 * (
        north_rows + south_rows - 2.0 * field
    )
    result = result - 0.25 * v_wind * (north_rows - south_rows)
    coriolis = jnp.concatenate(
        [turning * v_wind, -turning * u_wind, jnp.zeros_like(field[:, 2:])], axis=1
    )
    return result + coriolis


def local(state, courant, band_mask):
    levels, comps, cols, rows = state.shape
    lat_index = lax.axis_index("lat")
    lat_count = lax.axis_size("lat")
    z_index = lax.axis_index("lz")
    z_count = lax.axis_size("lz")
    assert z_count % 2 == 0 and ITERS == 2
    half_cycle = axis_count(LON) // 2
    total_rows = rows * lat_count
    row_ids = lat_index * rows + jnp.arange(rows, dtype=jnp.int32)
    latitude = jnp.pi / 2 - (row_ids.astype(jnp.float32) + 0.5) * jnp.pi / total_rows
    turning = 0.5 * jnp.sin(latitude)
    inverse = 1.0 / (1.0 + courant)
    rate = courant * inverse
    steps, carried = block_rates(rate)
    gain = carried[:, -1, :]
    band = band_mask == 1
    in_band = band[None, None, None, :]

    edge_rates = jnp.stack([rate[:, 0, :], inverse[:, 0, :]], axis=1)
    got_east = from_behind(jnp.concatenate([state[:, :, 0, :], edge_rates], axis=1), LON, -1)
    east, east_rates = got_east[:, :comps], got_east[:, comps:]
    west = from_behind(state[:, :, -1, :], LON, 1)
    north, south = lat_exchange(state[..., 0], state[..., -1], lat_index, half_cycle)
    star = state + stencil(state, north, south, east, west, turning)
    star_east = from_behind(star[:, :, 0, :], LON, -1)
    star_west = from_behind(star[:, :, -1, :], LON, 1)
    partial = block_scan(steps, star * inverse[:, None])
    own = (gain, partial[:, :, -1, :])
    entry = lon_inflow(own)
    estimate = jnp.where(in_band, partial + carried[:, None] * entry[:, :, None, :], star)

    band_col = band[None, None, :]
    west = 0.5 * (west + jnp.where(band_col, entry, star_west))
    carry_in = estimate[:, :, -1, :]
    east_value = east_rates[:, 0:1] * carry_in + east_rates[:, 1:2] * star_east
    east = 0.5 * (east + jnp.where(band_col, east_value, star_east))
    middle = 0.5 * (state + estimate)
    north, south = lat_exchange(middle[..., 0], middle[..., -1], lat_index, half_cycle)

    for sweep in range(1, ITERS):
        star = state + stencil(middle, north, south, east, west, turning)
        partial = block_scan(steps, star * inverse[:, None])
        own = (gain, partial[:, :, -1, :])
        entry = lon_inflow(own)
        estimate = jnp.where(in_band, partial + carried[:, None] * entry[:, :, None, :], star)
    return estimate


def solution(mesh):
    lon_count = mesh.shape["lon"]
    inner = 4
    split = Mesh(
        mesh.devices.reshape(lon_count // (inner * inner), inner, inner, mesh.shape["lat"]),
        ("lz", "lx", "lyc", "lat"),
    )
    in_specs = (P(None, None, LON, "lat"), P(None, LON, "lat"), P("lat"))
    out_specs = P(None, None, LON, "lat")
    return jax.shard_map(local, mesh=split, in_specs=in_specs, out_specs=out_specs, check_vma=False)
```

```python
import jax
import jax.numpy as jnp
from jax import lax
from jax.sharding import Mesh, PartitionSpec as P

ITERS = 2
LON = ("lz", "lx", "lyc")
GROUP = ("lx", "lyc")


def axis_count(axis):
    names = axis if isinstance(axis, tuple) else (axis,)
    count = 1
    for name in names:
        count *= lax.axis_size(name)
    return count


def from_behind(value, axis, steps):
    count = axis_count(axis)
    pairs = [(source, (source + steps) % count) for source in range(count)]
    return lax.ppermute(value, axis, pairs)


def shift_along(x, steps, axis, fill):
    pad_shape = list(x.shape)
    pad_shape[axis] = steps
    head = jnp.full(pad_shape, fill, x.dtype)
    body = lax.slice_in_dim(x, 0, x.shape[axis] - steps, axis=axis)
    return jnp.concatenate([head, body], axis=axis)


def block_rates(rate):
    steps = []
    span = 1
    while span < rate.shape[1]:
        steps.append((span, rate))
        rate = rate * shift_along(rate, span, 1, 1.0)
        span *= 2
    return steps, rate


def block_scan(steps, source):
    for span, rate in steps:
        source = source + rate[:, None] * shift_along(source, span, 2, 0.0)
    return source


def compose(later, earlier):
    return (later[0] * earlier[0], later[0][:, None] * earlier[1] + later[1])


def gathered(maps, axis):
    count = axis_count(axis)
    packed = jnp.concatenate([maps[1], maps[0][:, None]], axis=1)
    spread = jnp.broadcast_to(packed[None], (count,) + packed.shape)
    got = lax.all_to_all(spread, axis, 0, 0, tiled=False)
    return [(got[i][:, -1], got[i][:, :-1]) for i in range(count)]


def pick(options, index):
    rate, offset = options[0]
    for number in range(1, len(options)):
        chosen = index == number
        rate = jnp.where(chosen, options[number][0], rate)
        offset = jnp.where(chosen, options[number][1], offset)
    return rate, offset


def group_parts(members, index):
    count = len(members)
    ident = (jnp.ones_like(members[0][0]), jnp.zeros_like(members[0][1]))
    before = [ident]
    for i in range(1, count):
        before.append(compose(members[i - 1], before[-1]))
    after = [ident]
    for i in range(count - 2, -1, -1):
        after.insert(0, compose(after[0], members[i + 1]))
    total = compose(members[-1], before[-1])
    return total, pick(before, index), pick(after, index)


def cyclic_rest(members, index):
    count = len(members)
    options = []
    for g in range(count):
        rest = members[(g + 1) % count]
        for k in range(2, count):
            rest = compose(members[(g + k) % count], rest)
        options.append(rest)
    return pick(options, index)


def fixed_point(excl, own):
    rate, offset = own
    return (excl[0][:, None] * offset + excl[1]) / (1.0 - excl[0] * rate)[:, None]


def group_place():
    return lax.axis_index("lx") * lax.axis_size("lyc") + lax.axis_index("lyc")


def lon_inflow(own):
    total, before, after = group_parts(gathered(own, GROUP), group_place())
    rest = cyclic_rest(gathered(total, "lz"), lax.axis_index("lz"))
    return fixed_point(compose(before, compose(rest, after)), own)


def lat_exchange(top, bottom, lat_index, half_cycle):
    lon_count = axis_count(LON)
    lat_count = lax.axis_size("lat")
    assert lat_count % 2 == 0
    odd = lat_index % 2 == 1
    pairs_a = []
    pairs_b = []
    for d in range(lon_count):
        for l in range(lat_count):
            me = d * lat_count + l
            if l % 2 == 0:
                pairs_a.append((me, d * lat_count + l + 1))
            else:
                pairs_a.append((me, d * lat_count + l - 1))
            if l == 0 or l == lat_count - 1:
                pairs_b.append((me, ((d + half_cycle) % lon_count) * lat_count + l))
            elif l % 2 == 1:
                pairs_b.append((me, d * lat_count + l + 1))
            else:
                pairs_b.append((me, d * lat_count + l - 1))
    got_a = lax.ppermute(jnp.where(odd, top, bottom), LON + ("lat",), pairs_a)
    got_b = lax.ppermute(jnp.where(odd, bottom, top), LON + ("lat",), pairs_b)
    pole = (lat_index == 0) | (lat_index == lat_count - 1)
    got_b = jnp.where(pole, got_b * flips()[None, :, None], got_b)
    return jnp.where(odd, got_a, got_b), jnp.where(odd, got_b, got_a)


def flips():
    return jnp.array([-1.0, -1.0, 1.0, 1.0], jnp.float32)


def stencil(field, north, south, east, west, turning):
    north_rows = jnp.concatenate([north[..., None], field[..., :-1]], axis=3)
    south_rows = jnp.concatenate([field[..., 1:], south[..., None]], axis=3)
    east_cells = jnp.concatenate([field[:, :, 1:], east[:, :, None]], axis=2)
    west_cells = jnp.concatenate([west[:, :, None], field[:, :, :-1]], axis=2)
    u_wind = field[:, 0:1]
    v_wind = field[:, 1:2]
    result = 0.1 * (east_cells + west_cells - 2.0 * field) + 0.1 * (
        north_rows + south_rows - 2.0 * field
    )
    result = result - 0.25 * v_wind * (north_rows - south_rows)
    coriolis = jnp.concatenate(
        [turning * v_wind, -turning * u_wind, jnp.zeros_like(field[:, 2:])], axis=1
    )
    return result + coriolis


def column_star(field, east, west, north_end, south_end, turning):
    north_rows = jnp.concatenate([north_end[..., None], field[..., :-1]], axis=-1)
    south_rows = jnp.concatenate([field[..., 1:], south_end[..., None]], axis=-1)
    u_wind = field[:, 0:1]
    v_wind = field[:, 1:2]
    result = 0.1 * (east + west - 2.0 * field) + 0.1 * (north_rows + south_rows - 2.0 * field)
    result = result - 0.25 * v_wind * (north_rows - south_rows)
    coriolis = jnp.concatenate(
        [turning * v_wind, -turning * u_wind, jnp.zeros_like(field[:, 2:])], axis=1
    )
    return field + (result + coriolis)


def local(state, courant, band_mask):
    levels, comps, cols, rows = state.shape
    lat_index = lax.axis_index("lat")
    lat_count = lax.axis_size("lat")
    z_index = lax.axis_index("lz")
    z_count = lax.axis_size("lz")
    assert z_count % 2 == 0 and ITERS == 2
    half_cycle = axis_count(LON) // 2
    total_rows = rows * lat_count
    row_ids = lat_index * rows + jnp.arange(rows, dtype=jnp.int32)
    latitude = jnp.pi / 2 - (row_ids.astype(jnp.float32) + 0.5) * jnp.pi / total_rows
    turning = 0.5 * jnp.sin(latitude)
    inverse = 1.0 / (1.0 + courant)
    rate = courant * inverse
    steps, carried = block_rates(rate)
    gain = carried[:, -1, :]
    band = band_mask == 1
    in_band = band[None, None, None, :]

    edge_rates = jnp.stack([rate[:, 0, :], inverse[:, 0, :]], axis=1)
    east_message = jnp.concatenate([state[:, :, 0, :], state[:, :, 1, :], edge_rates], axis=1)
    got_east = from_behind(east_message, LON, -1)
    east, east_next = got_east[:, :comps], got_east[:, comps:2 * comps]
    east_rates = got_east[:, 2 * comps:]
    got_west = from_behind(jnp.concatenate([state[:, :, -1, :], state[:, :, -2, :]], axis=1), LON, 1)
    west, west_next = got_west[:, :comps], got_west[:, comps:]
    north, south = lat_exchange(state[..., 0], state[..., -1], lat_index, half_cycle)
    star = state + stencil(state, north, south, east, west, turning)
    partial = block_scan(steps, star * inverse[:, None])
    own = (gain, partial[:, :, -1, :])
    entry = lon_inflow(own)
    estimate = jnp.where(in_band, partial + carried[:, None] * entry[:, :, None, :], star)

    middle = 0.5 * (state + estimate)
    top = jnp.concatenate([middle[..., 0], east[..., 0][..., None], west[..., 0][..., None]], axis=2)
    bottom = jnp.concatenate(
        [middle[..., -1], east[..., -1][..., None], west[..., -1][..., None]], axis=2
    )
    got_north, got_south = lat_exchange(top, bottom, lat_index, half_cycle)
    star_east = column_star(
        east, east_next, state[:, :, -1, :], got_north[..., cols], got_south[..., cols], turning
    )
    star_west = column_star(
        west, state[:, :, 0, :], west_next, got_north[..., cols + 1], got_south[..., cols + 1], turning
    )

    band_col = band[None, None, :]
    west = 0.5 * (west + jnp.where(band_col, entry, star_west))
    carry_in = estimate[:, :, -1, :]
    east_value = east_rates[:, 0:1] * carry_in + east_rates[:, 1:2] * star_east
    east = 0.5 * (east + jnp.where(band_col, east_value, star_east))
    north, south = got_north[..., :cols], got_south[..., :cols]

    for sweep in range(1, ITERS):
        star = state + stencil(middle, north, south, east, west, turning)
        partial = block_scan(steps, star * inverse[:, None])
        own = (gain, partial[:, :, -1, :])
        entry = lon_inflow(own)
        estimate = jnp.where(in_band, partial + carried[:, None] * entry[:, :, None, :], star)
    return estimate


def solution(mesh):
    lon_count = mesh.shape["lon"]
    inner = 4
    split = Mesh(
        mesh.devices.reshape(lon_count // (inner * inner), inner, inner, mesh.shape["lat"]),
        ("lz", "lx", "lyc", "lat"),
    )
    in_specs = (P(None, None, LON, "lat"), P(None, LON, "lat"), P("lat"))
    out_specs = P(None, None, LON, "lat")
    return jax.shard_map(local, mesh=split, in_specs=in_specs, out_specs=out_specs, check_vma=False)
```
